256 devices in a mesh: term: 4 (over x), sec: 64 (over y, z, core).
Axes of the slice: x: 4, y: 4, z: 8, core: 2. Of those that a mesh axis runs over, the one named last changes fastest.
Arguments:
- vectors: bfloat16 [1, 4096, 256, 256], P(None, 'sec'), may hold values from -6 to 6
- left_env: bfloat16 [4, 128, 256, 256], P('term', 'sec'), may hold values from -0.375 to 0.375
- right_env: bfloat16 [4, 128, 256, 256], P('term', 'sec'), may hold values from -0.375 to 0.375
- left_sector: int32 [64, 64], P('sec'), may hold values from 0 to 1
- right_sector: int32 [64, 64], P('sec'), may hold values from 0 to 1
- tile_count: int32 [64], P('sec'), may hold values from 1 to 64, 3072 in all
- departure: int32 [64, 64], P('sec'), may hold values from 0 to 63, each once within a row
- arrival: int32 [64, 64], P('sec'), may hold values from 0 to 63, each once within a row
Outputs:
- sigma: bfloat16 [1, 4096, 256, 256], P(None, 'sec', 'term')
The draws below stay inside these ranges and needn't reach their ends.
Inputs may be any that keep to these rules, and one draw needn't show every extreme that they name: `tile_count`: every sec index owns some tile slots that are live; the busiest left owner has all 64 slots live. `departure`: each row is a permutation of the slots. `arrival`: each row is a permutation of the slots.
All inputs are finite; a program needn't handle non-finite values. No bound on the sum of `tile_count` on one device may be relied on, other than what follows from the above.
Results may differ from the reference program's by a relative error of at most 0.015.
Values may be sent and summed in bfloat16 or wider, within the bound.
No kernel may reach another device: no remote copies, remote signals or barrier semaphores. Data moves between devices by JAX's collectives and lax.ppermute only.
A program may use at most 128 MiB of HBM per device.

```python
import math
import jax
import jax.numpy as jnp
import numpy as np
from jax import lax

W = 256
SEC_DEV = 2
VECS = 1
TILES_DEV = 64
TILES = 4096
SECTORS = 128
TERMS = 4
N_SEC = 64


def plant(values, stream_key, smallest, largest):
    shape = values.shape
    spot = [jax.random.randint(jax.random.fold_in(stream_key, axis), (), 0, shape[axis]) for axis in range(len(shape))]
    values = values.at[tuple(spot)].set(smallest)
    longest = shape.index(max(shape))
    spot[longest] = (spot[longest] + 1) % shape[longest]
    return values.at[tuple(spot)].set(largest)


def shard_levels(rng, extent, split, low, largest):
    def one(dim, parts):
        draws = jax.random.uniform(jax.random.fold_in(jax.random.fold_in(rng, 6), dim), (parts,), jnp.float32, low / len(split), largest / len(split))
        return jnp.repeat(jnp.exp(draws), extent[dim] // parts).reshape((-1,) + (1,) * (len(extent) - dim - 1))

    level = one(*split[0])
    for cut in split[1:]:
        level = level * one(*cut)
    return level


def profile(number_of, total, most, skew):
    portions = [(1 << 20) // math.isqrt(standing ** skew) + 1 for standing in range(2, number_of + 1)]
    rest, given = total - most - (number_of - 1), [1] * (number_of - 1)
    while rest > 0:
        free = [i for i in range(number_of - 1) if given[i] < most]
        pool, remaining = sum([portions[i] for i in free]), rest
        for i in free:
            addition = min(most - given[i], max(1, remaining * portions[i] // pool), rest)
            given[i] = given[i] + addition
            rest = rest - addition
    return np.array([most] + given)


def uneven(stream_key, amount, total, most, skew):
    if amount == 2:
        one = jax.random.randint(stream_key, (), max(1, total - most), min(most, total - 1) + 1)
        return jnp.stack([one, total - one])
    tallies = jnp.asarray(profile(amount, total, most, skew), jnp.int32)
    twos = (amount - 1) // 2
    source_of, receiver = tallies[1:1 + 2 * twos:2], tallies[2:2 + 2 * twos:2]
    room = jnp.minimum(source_of - 1, most - receiver)
    moved = jax.random.randint(jax.random.fold_in(stream_key, 1), (twos,), 0, 1 << 20) % (room + 1)
    tallies = tallies.at[1:1 + 2 * twos:2].set(source_of - moved).at[2:2 + 2 * twos:2].set(receiver + moved)
    return tallies[jax.random.permutation(jax.random.fold_in(stream_key, 2), amount)]


def normal_values(own_key, dims, spread, most, split=(), kind=jnp.bfloat16):
    drawn = spread * jax.random.normal(own_key, dims, jnp.float32)
    if split:
        drawn = drawn * shard_levels(own_key, dims, split, -0.22, 0.18)
    return jnp.clip(drawn, -most, most).astype(kind)


def setup_inputs(seed: int = 0) -> dict:
    splits = jax.random.split(jax.random.key(seed), 9)
    return {
        "vectors": normal_values(splits[0], (VECS, TILES, W, W), 1.0, 6.0, ((1, 64),)),
        "left_env": normal_values(splits[1], (TERMS, SECTORS, W, W), W ** -0.5, 0.375, ((0, 4), (1, 64))),
        "right_env": normal_values(splits[2], (TERMS, SECTORS, W, W), W ** -0.5, 0.375, ((0, 4), (1, 64))),
        "left_sector": plant(jax.random.randint(splits[3], (N_SEC, TILES_DEV), 0, SEC_DEV), jax.random.fold_in(splits[3], 1), 0, SEC_DEV - 1).astype(jnp.int32),
        "right_sector": plant(jax.random.randint(splits[4], (N_SEC, TILES_DEV), 0, SEC_DEV), jax.random.fold_in(splits[4], 1), 0, SEC_DEV - 1).astype(jnp.int32),
        "tile_count": uneven(splits[5], N_SEC, N_SEC * TILES_DEV * 3 // 4, TILES_DEV, 2).astype(jnp.int32),
        "departure": jax.vmap(lambda own: jax.random.permutation(own, TILES_DEV))(jax.random.split(splits[6], N_SEC)).reshape((N_SEC, TILES_DEV)).astype(jnp.int32),
        "arrival": jax.vmap(lambda own: jax.random.permutation(own, TILES_DEV))(jax.random.split(splits[7], N_SEC)).reshape((N_SEC, TILES_DEV)).astype(jnp.int32),
    }


def reference(vectors, left_env, right_env, left_sector, right_sector, tile_count, departure, arrival):
    per_peer = TILES_DEV // N_SEC

    def one_owner(owner):
        arrive = arrival[owner]
        source = arrive // per_peer
        position = owner * per_peer + arrive % per_peer
        left_slot = departure[source, position]
        live = left_slot < tile_count[source]
        left_global = source * SEC_DEV + left_sector[source, left_slot]
        right_global = owner * SEC_DEV + right_sector[owner]
        tiles = vectors[:, source * TILES_DEV + left_slot]
        tiles = jnp.where(live[None, :, None, None], tiles, jnp.zeros_like(tiles))
        left_blocks = left_env[:, left_global]
        right_blocks = right_env[:, right_global]
        applied = jnp.einsum("tkij,vkjl->tvkil", left_blocks.astype(jnp.float32), tiles.astype(jnp.float32)).astype(jnp.bfloat16)
        contrib = jnp.einsum("tvkil,tkml->tvkim", applied.astype(jnp.float32), right_blocks.astype(jnp.float32)).astype(jnp.bfloat16)
        return jnp.sum(contrib.astype(jnp.float32), axis=0).astype(jnp.bfloat16)

    result = lax.map(one_owner, jnp.arange(N_SEC, dtype=jnp.int32))
    result = jnp.transpose(result, (1, 0, 2, 3, 4))
    return result.reshape(VECS, TILES, W, W)
```

```python
import functools

import jax
import jax.numpy as jnp
from jax import lax
from jax.experimental import pallas as pl
from jax.experimental.pallas import tpu as pltpu
from jax.sharding import PartitionSpec as P

CHUNK = 8
VMEM_LIMIT = 48 * 1024 * 1024


def _left_kernel(dep_ref, lsel_ref, live_ref, m_ref, x_ref, o_ref):
    base = pl.program_id(0) * CHUNK
    for k in range(CHUNK):
        e = base + k
        prod = jnp.dot(
            m_ref[lsel_ref[e]], x_ref[dep_ref[e]], preferred_element_type=jnp.float32
        )
        o_ref[k] = jnp.where(live_ref[e] > 0, prod, 0.0).astype(o_ref.dtype)


def apply_left(stacked, tiles, dep, lsel, live):
    n, w, _ = tiles.shape
    spec = pltpu.PrefetchScalarGridSpec(
        num_scalar_prefetch=3,
        grid=(n // CHUNK,),
        in_specs=[
            pl.BlockSpec(stacked.shape, lambda c, *_: (0, 0, 0)),
            pl.BlockSpec(tiles.shape, lambda c, *_: (0, 0, 0)),
        ],
        out_specs=pl.BlockSpec((CHUNK, w, w), lambda c, *_: (c, 0, 0)),
    )
    return pl.pallas_call(
        _left_kernel,
        grid_spec=spec,
        out_shape=jax.ShapeDtypeStruct((n, stacked.shape[1], w), jnp.bfloat16),
        compiler_params=pltpu.CompilerParams(vmem_limit_bytes=VMEM_LIMIT),
        cost_estimate=pl.CostEstimate(
            flops=2 * n * stacked.shape[1] * w * w,
            bytes_accessed=2 * (2 * n * w * w + stacked.size),
            transcendentals=0,
        ),
    )(dep, lsel, live, stacked, tiles)


def _right_kernel(n_term, arr_ref, rsel_ref, a_ref, r_ref, o_ref):
    base = pl.program_id(0) * CHUNK
    rows = o_ref.shape[1]
    for k in range(CHUNK):
        s = base + k
        block = a_ref[arr_ref[s]]
        sector = rsel_ref[s]
        acc = None
        for tp in range(n_term):
            part = lax.dot_general(
                block[tp * rows:(tp + 1) * rows],
                r_ref[tp * 2 + sector],
                (((1,), (1,)), ((), ())),
                preferred_element_type=jnp.float32,
            )
            acc = part if acc is None else acc + part
        o_ref[k] = acc.astype(o_ref.dtype)


def apply_right(placed, right_all, arr, rsel, n_term):
    n, height, w = placed.shape
    rows = height // n_term
    spec = pltpu.PrefetchScalarGridSpec(
        num_scalar_prefetch=2,
        grid=(n // CHUNK,),
        in_specs=[
            pl.BlockSpec(placed.shape, lambda c, *_: (0, 0, 0)),
            pl.BlockSpec(right_all.shape, lambda c, *_: (0, 0, 0)),
        ],
        out_specs=pl.BlockSpec((CHUNK, rows, w), lambda c, *_: (c, 0, 0)),
    )
    return pl.pallas_call(
        functools.partial(_right_kernel, n_term),
        grid_spec=spec,
        out_shape=jax.ShapeDtypeStruct((n, rows, w), jnp.bfloat16),
        compiler_params=pltpu.CompilerParams(vmem_limit_bytes=VMEM_LIMIT),
        cost_estimate=pl.CostEstimate(
            flops=2 * n * height * w * w,
            bytes_accessed=2 * (n * height * w + right_all.size + n * rows * w),
            transcendentals=0,
        ),
    )(arr, rsel, placed, right_all)


def on_device(
    vectors, left_env, right_env, left_sector, right_sector, tile_count, departure, arrival
):
    n_term = lax.axis_size("term")
    n_vecs, tiles_dev, width, _ = vectors.shape
    n_sec_local = left_env.shape[1]
    rows = width // n_term

    left_rows = lax.all_to_all(
        left_env[0].reshape(n_sec_local, n_term, rows, width),
        "term", split_axis=1, concat_axis=1, tiled=True,
    )
    stacked = left_rows.reshape(n_sec_local, n_term * rows, width)

    right_all = lax.all_to_all(
        jnp.broadcast_to(right_env, (n_term,) + right_env.shape[1:]),
        "term", split_axis=0, concat_axis=0, tiled=True,
    ).reshape(n_term * n_sec_local, width, width)

    dep = departure[0]
    lsel = jnp.take(left_sector[0], dep)
    live = (dep < tile_count[0]).astype(jnp.int32)
    arr = arrival[0]
    rsel = right_sector[0]

    outs = []
    for v in range(n_vecs):
        outgoing = apply_left(stacked, vectors[v], dep, lsel, live)
        incoming = lax.all_to_all(outgoing, "sec", split_axis=0, concat_axis=0, tiled=True)
        outs.append(apply_right(incoming, right_all, arr, rsel, n_term))
    return jnp.stack(outs)


def solution(mesh):
    in_specs = (
        P(None, "sec", None, None),
        P("term", "sec", None, None),
        P("term", "sec", None, None),
        P("sec", None),
        P("sec", None),
        P("sec"),
        P("sec", None),
        P("sec", None),
    )
    out_specs = P(None, "sec", "term", None)
    return jax.shard_map(
        on_device, mesh=mesh, in_specs=in_specs, out_specs=out_specs, check_vma=False
    )
```

```python
import functools

import jax
import jax.numpy as jnp
from jax import lax
from jax.experimental import pallas as pl
from jax.experimental.pallas import tpu as pltpu
from jax.sharding import PartitionSpec as P

CHUNK = 8
VMEM_LIMIT = 48 * 1024 * 1024


def _left_kernel(dep_ref, lsel_ref, live_ref, idx_ref, l_ref, x_ref, o_ref):
    base = pl.program_id(0) * CHUNK
    for k in range(CHUNK):
        e = base + k
        prod = jnp.dot(
            l_ref[lsel_ref[e], 0], x_ref[dep_ref[e]], preferred_element_type=jnp.float32
        )
        o_ref[k] = jnp.where(live_ref[e] > 0, prod, 0.0).astype(o_ref.dtype)


def apply_left(slabs, tiles, dep, lsel, live, idx):
    n, w, _ = tiles.shape
    n_sector, _, rows, _ = slabs.shape
    spec = pltpu.PrefetchScalarGridSpec(
        num_scalar_prefetch=4,
        grid=(n // CHUNK,),
        in_specs=[
            pl.BlockSpec((n_sector, 1, rows, w), lambda c, d, s, v, i: (0, i[0], 0, 0)),
            pl.BlockSpec(tiles.shape, lambda c, *_: (0, 0, 0)),
        ],
        out_specs=pl.BlockSpec((CHUNK, rows, w), lambda c, *_: (c, 0, 0)),
    )
    return pl.pallas_call(
        _left_kernel,
        grid_spec=spec,
        out_shape=jax.ShapeDtypeStruct((n, rows, w), jnp.bfloat16),
        compiler_params=pltpu.CompilerParams(vmem_limit_bytes=VMEM_LIMIT),
        cost_estimate=pl.CostEstimate(
            flops=2 * n * rows * w * w,
            bytes_accessed=2 * (n * w * w + n * rows * w),
            transcendentals=0,
        ),
    )(dep, lsel, live, idx, slabs, tiles)


def _right_kernel(accumulate, arr_ref, rsel_ref, idx_ref, a_ref, r_ref, *rest):
    if accumulate:
        acc_ref, o_ref = rest
    else:
        (o_ref,) = rest
    base = pl.program_id(0) * CHUNK
    for k in range(CHUNK):
        s = base + k
        part = lax.dot_general(
            a_ref[arr_ref[s]],
            r_ref[0, rsel_ref[s]],
            (((1,), (1,)), ((), ())),
            preferred_element_type=jnp.float32,
        )
        if accumulate:
            part = part + acc_ref[k]
        o_ref[k] = part.astype(o_ref.dtype)


def apply_right(placed, blocks, arr, rsel, idx, acc, out_dtype):
    n, rows, w = placed.shape
    n_sector = blocks.shape[1]
    in_specs = [
        pl.BlockSpec(placed.shape, lambda c, *_: (0, 0, 0)),
        pl.BlockSpec((1, n_sector, w, w), lambda c, a, r, i: (i[0], 0, 0, 0)),
    ]
    operands = [arr, rsel, idx, placed, blocks]
    aliases = {}
    if acc is not None:
        in_specs.append(pl.BlockSpec((CHUNK, rows, w), lambda c, *_: (c, 0, 0)))
        operands.append(acc)
        if acc.dtype == out_dtype:
            aliases = {5: 0}
    spec = pltpu.PrefetchScalarGridSpec(
        num_scalar_prefetch=3,
        grid=(n // CHUNK,),
        in_specs=in_specs,
        out_specs=pl.BlockSpec((CHUNK, rows, w), lambda c, *_: (c, 0, 0)),
    )
    return pl.pallas_call(
        functools.partial(_right_kernel, acc is not None),
        grid_spec=spec,
        out_shape=jax.ShapeDtypeStruct((n, rows, w), out_dtype),
        input_output_aliases=aliases,
        compiler_params=pltpu.CompilerParams(vmem_limit_bytes=VMEM_LIMIT),
        cost_estimate=pl.CostEstimate(
            flops=2 * n * rows * w * w,
            bytes_accessed=2 * n * rows * w + 2 * n_sector * w * w + 8 * n * rows * w,
            transcendentals=0,
        ),
    )(*operands)


def on_device(
    vectors, left_env, right_env, left_sector, right_sector, tile_count, departure, arrival
):
    n_term = lax.axis_size("term")
    me = lax.axis_index("term")
    n_vecs, tiles_dev, width, _ = vectors.shape
    n_sector = left_env.shape[1]
    rows = width // n_term

    own_left = left_env[0].reshape(n_sector, n_term, rows, width)
    left_rows = lax.all_to_all(own_left, "term", split_axis=1, concat_axis=1, tiled=True)
    right_all = lax.all_to_all(
        jnp.broadcast_to(right_env, (n_term,) + right_env.shape[1:]),
        "term", split_axis=0, concat_axis=0, tiled=True,
    )

    dep = departure[0]
    lsel = jnp.take(left_sector[0], dep)
    live = (dep < tile_count[0]).astype(jnp.int32)
    arr = arrival[0]
    rsel = right_sector[0]

    outs = []
    for v in range(n_vecs):
        acc = None
        for c in range(n_term):
            term = (me + c) % n_term
            if c == 0:
                slabs, lidx = own_left, me
                blocks, ridx = right_env, jnp.int32(0)
            else:
                slabs, lidx = left_rows, term
                blocks, ridx = right_all, term
            lidx = jnp.reshape(lidx, (1,)).astype(jnp.int32)
            ridx = jnp.reshape(ridx, (1,)).astype(jnp.int32)
            outgoing = apply_left(slabs, vectors[v], dep, lsel, live, lidx)
            incoming = lax.all_to_all(outgoing, "sec", split_axis=0, concat_axis=0, tiled=True)
            last = c == n_term - 1
            acc = apply_right(
                incoming, blocks, arr, rsel, ridx, acc,
                vectors.dtype if last else jnp.float32,
            )
        outs.append(acc)
    return jnp.stack(outs)


def solution(mesh):
    in_specs = (
        P(None, "sec", None, None),
        P("term", "sec", None, None),
        P("term", "sec", None, None),
        P("sec", None),
        P("sec", None),
        P("sec"),
        P("sec", None),
        P("sec", None),
    )
    out_specs = P(None, "sec", "term", None)
    return jax.shard_map(
        on_device, mesh=mesh, in_specs=in_specs, out_specs=out_specs, check_vma=False
    )
```

```python
import functools

import jax
import jax.numpy as jnp
from jax import lax
from jax.experimental import pallas as pl
from jax.experimental.pallas import tpu as pltpu
from jax.sharding import PartitionSpec as P

CHUNK = 8
VMEM_LIMIT = 48 * 1024 * 1024


def _left_kernel(dep_ref, sector_ref, count_ref, m_ref, x_ref, o_ref):
    base = pl.program_id(0) * CHUNK
    for k in range(CHUNK):
        slot = dep_ref[base + k]
        prod = jnp.dot(
            m_ref[sector_ref[slot]], x_ref[slot], preferred_element_type=jnp.float32
        )
        o_ref[k] = jnp.where(slot < count_ref[0], prod, 0.0).astype(o_ref.dtype)


def apply_left(stacked, tiles, dep, left_sector, tile_count):
    n, w, _ = tiles.shape
    height = stacked.shape[1]
    spec = pltpu.PrefetchScalarGridSpec(
        num_scalar_prefetch=3,
        grid=(n // CHUNK,),
        in_specs=[
            pl.BlockSpec(stacked.shape, lambda c, *_: (0, 0, 0)),
            pl.BlockSpec(tiles.shape, lambda c, *_: (0, 0, 0)),
        ],
        out_specs=pl.BlockSpec((CHUNK, height, w), lambda c, *_: (c, 0, 0)),
    )
    return pl.pallas_call(
        _left_kernel,
        grid_spec=spec,
        out_shape=jax.ShapeDtypeStruct((n, height, w), jnp.bfloat16),
        compiler_params=pltpu.CompilerParams(vmem_limit_bytes=VMEM_LIMIT),
        cost_estimate=pl.CostEstimate(
            flops=2 * n * height * w * w,
            bytes_accessed=2 * (n * w * w + n * height * w + stacked.size),
            transcendentals=0,
        ),
    )(dep, left_sector, tile_count, stacked, tiles)


def _right_kernel(n_term, n_sector, arr_ref, rsel_ref, a_ref, rt_ref, o_ref):
    base = pl.program_id(0) * CHUNK
    rows = o_ref.shape[1]
    accs = [None] * n_sector
    for p in range(n_term):
        lhs = jnp.concatenate(
            [a_ref[arr_ref[base + k], pl.ds(p * rows, rows), :] for k in range(CHUNK)],
            axis=0,
        )
        for sector in range(n_sector):
            part = jnp.dot(
                lhs, rt_ref[p * n_sector + sector], preferred_element_type=jnp.float32
            )
            accs[sector] = part if accs[sector] is None else accs[sector] + part
    for k in range(CHUNK):
        chosen = rsel_ref[base + k]
        out = accs[n_sector - 1][k * rows:(k + 1) * rows]
        for sector in range(n_sector - 1):
            out = jnp.where(chosen == sector, accs[sector][k * rows:(k + 1) * rows], out)
        o_ref[k] = out.astype(o_ref.dtype)


def apply_right(placed, right_t, arr, rsel, n_term, n_sector):
    n, height, w = placed.shape
    rows = height // n_term
    spec = pltpu.PrefetchScalarGridSpec(
        num_scalar_prefetch=2,
        grid=(n // CHUNK,),
        in_specs=[
            pl.BlockSpec(placed.shape, lambda c, *_: (0, 0, 0)),
            pl.BlockSpec(right_t.shape, lambda c, *_: (0, 0, 0)),
        ],
        out_specs=pl.BlockSpec((CHUNK, rows, w), lambda c, *_: (c, 0, 0)),
    )
    return pl.pallas_call(
        functools.partial(_right_kernel, n_term, n_sector),
        grid_spec=spec,
        out_shape=jax.ShapeDtypeStruct((n, rows, w), jnp.bfloat16),
        compiler_params=pltpu.CompilerParams(vmem_limit_bytes=VMEM_LIMIT),
        cost_estimate=pl.CostEstimate(
            flops=2 * n_sector * n * height * w * w,
            bytes_accessed=2 * (n * height * w + right_t.size + n * rows * w),
            transcendentals=0,
        ),
    )(arr, rsel, placed, right_t)


def on_device(
    vectors, left_env, right_env, left_sector, right_sector, tile_count, departure, arrival
):
    n_term = lax.axis_size("term")
    me = lax.axis_index("term")
    n_vecs, tiles_dev, width, _ = vectors.shape
    n_sector = left_env.shape[1]
    rows = width // n_term

    own_left = left_env[0]
    own_right_t = jnp.swapaxes(right_env[0], 1, 2)
    left_parts = [lax.dynamic_slice_in_dim(own_left, me * rows, rows, axis=1)]
    right_parts = [own_right_t]
    for k in range(1, n_term):
        perm = [(i, (i + k) % n_term) for i in range(n_term)]
        dest = (me + k) % n_term
        send = lax.dynamic_slice_in_dim(own_left, dest * rows, rows, axis=1)
        left_parts.append(lax.ppermute(send, "term", perm))
        right_parts.append(lax.ppermute(own_right_t, "term", perm))
    stacked = jnp.concatenate(left_parts, axis=1)
    right_t = jnp.stack(right_parts).reshape(n_term * n_sector, width, width)

    outs = []
    for v in range(n_vecs):
        outgoing = apply_left(stacked, vectors[v], departure[0], left_sector[0], tile_count)
        incoming = lax.all_to_all(outgoing, "sec", split_axis=0, concat_axis=0, tiled=True)
        outs.append(apply_right(incoming, right_t, arrival[0], right_sector[0], n_term, n_sector))
    return jnp.stack(outs)


def solution(mesh):
    in_specs = (
        P(None, "sec", None, None),
        P("term", "sec", None, None),
        P("term", "sec", None, None),
        P("sec", None),
        P("sec", None),
        P("sec"),
        P("sec", None),
        P("sec", None),
    )
    out_specs = P(None, "sec", "term", None)
    return jax.shard_map(
        on_device, mesh=mesh, in_specs=in_specs, out_specs=out_specs, check_vma=False
    )
```

```python
import functools

import jax
import jax.numpy as jnp
from jax import lax
from jax.experimental import pallas as pl
from jax.experimental.pallas import tpu as pltpu
from jax.sharding import PartitionSpec as P

CHUNK = 8
VMEM_LIMIT = 48 * 1024 * 1024


def _left_kernel(dep_ref, sector_ref, count_ref, m_ref, x_ref, o_ref):
    base = pl.program_id(0) * CHUNK
    n_term, _, rows, _ = o_ref.shape
    for k in range(CHUNK):
        slot = dep_ref[base + k]
        prod = jnp.dot(
            m_ref[sector_ref[slot]], x_ref[slot], preferred_element_type=jnp.float32
        )
        prod = jnp.where(slot < count_ref[0], prod, 0.0).astype(o_ref.dtype)
        for p in range(n_term):
            o_ref[p, k] = prod[p * rows:(p + 1) * rows]


def apply_left(blocks, tiles, dep, left_sector, tile_count, n_term):
    n, w, _ = tiles.shape
    rows = w // n_term
    spec = pltpu.PrefetchScalarGridSpec(
        num_scalar_prefetch=3,
        grid=(n // CHUNK,),
        in_specs=[
            pl.BlockSpec(blocks.shape, lambda c, *_: (0, 0, 0)),
            pl.BlockSpec(tiles.shape, lambda c, *_: (0, 0, 0)),
        ],
        out_specs=pl.BlockSpec((n_term, CHUNK, rows, w), lambda c, *_: (0, c, 0, 0)),
    )
    return pl.pallas_call(
        _left_kernel,
        grid_spec=spec,
        out_shape=jax.ShapeDtypeStruct((n_term, n, rows, w), jnp.bfloat16),
        compiler_params=pltpu.CompilerParams(vmem_limit_bytes=VMEM_LIMIT),
        cost_estimate=pl.CostEstimate(
            flops=2 * n * w * w * w,
            bytes_accessed=2 * (2 * n * w * w + blocks.size),
            transcendentals=0,
        ),
    )(dep, left_sector, tile_count, blocks, tiles)


def _right_kernel(n_term, n_sector, arr_ref, rsel_ref, me_ref, a_ref, rt_ref, o_ref):
    base = pl.program_id(0) * CHUNK
    rows = o_ref.shape[1]
    per_term = a_ref.shape[0] // n_term
    accs = [None] * n_sector
    for k in range(n_term):
        origin = lax.rem(me_ref[0] + (n_term - k), n_term) * per_term
        lhs = jnp.concatenate(
            [a_ref[origin + arr_ref[base + q]] for q in range(CHUNK)], axis=0
        )
        for sector in range(n_sector):
            part = jnp.dot(
                lhs, rt_ref[k * n_sector + sector], preferred_element_type=jnp.float32
            )
            accs[sector] = part if accs[sector] is None else accs[sector] + part
    for q in range(CHUNK):
        chosen = rsel_ref[base + q]
        out = accs[n_sector - 1][q * rows:(q + 1) * rows]
        for sector in range(n_sector - 1):
            out = jnp.where(chosen == sector, accs[sector][q * rows:(q + 1) * rows], out)
        o_ref[q] = out.astype(o_ref.dtype)


def apply_right(incoming, right_t, arr, rsel, me, n_term, n_sector):
    total, rows, w = incoming.shape
    n = arr.shape[0]
    spec = pltpu.PrefetchScalarGridSpec(
        num_scalar_prefetch=3,
        grid=(n // CHUNK,),
        in_specs=[
            pl.BlockSpec(incoming.shape, lambda c, *_: (0, 0, 0)),
            pl.BlockSpec(right_t.shape, lambda c, *_: (0, 0, 0)),
        ],
        out_specs=pl.BlockSpec((CHUNK, rows, w), lambda c, *_: (c, 0, 0)),
    )
    return pl.pallas_call(
        functools.partial(_right_kernel, n_term, n_sector),
        grid_spec=spec,
        out_shape=jax.ShapeDtypeStruct((n, rows, w), jnp.bfloat16),
        compiler_params=pltpu.CompilerParams(vmem_limit_bytes=VMEM_LIMIT),
        cost_estimate=pl.CostEstimate(
            flops=2 * n_sector * total * rows * w * w,
            bytes_accessed=2 * (total * rows * w + right_t.size + n * rows * w),
            transcendentals=0,
        ),
    )(arr, rsel, me, incoming, right_t)


def on_device(
    vectors, left_env, right_env, left_sector, right_sector, tile_count, departure, arrival
):
    n_term = lax.axis_size("term")
    me = lax.axis_index("term")
    n_vecs, tiles_dev, width, _ = vectors.shape
    n_sector = left_env.shape[1]
    rows = width // n_term

    own_right_t = jnp.swapaxes(right_env[0], 1, 2)
    right_parts = [own_right_t]
    for k in range(1, n_term):
        perm = [(i, (i + k) % n_term) for i in range(n_term)]
        right_parts.append(lax.ppermute(own_right_t, "term", perm))
    right_t = jnp.stack(right_parts).reshape(n_term * n_sector, width, width)
    me_arr = jnp.reshape(me, (1,)).astype(jnp.int32)

    outs = []
    for v in range(n_vecs):
        outgoing = apply_left(
            left_env[0], vectors[v], departure[0], left_sector[0], tile_count, n_term
        )
        incoming = lax.all_to_all(
            outgoing.reshape(n_term * tiles_dev, rows, width),
            ("term", "sec"), split_axis=0, concat_axis=0, tiled=True,
        )
        outs.append(
            apply_right(incoming, right_t, arrival[0], right_sector[0], me_arr, n_term, n_sector)
        )
    return jnp.stack(outs)


def solution(mesh):
    in_specs = (
        P(None, "sec", None, None),
        P("term", "sec", None, None),
        P("term", "sec", None, None),
        P("sec", None),
        P("sec", None),
        P("sec"),
        P("sec", None),
        P("sec", None),
    )
    out_specs = P(None, "sec", "term", None)
    return jax.shard_map(
        on_device, mesh=mesh, in_specs=in_specs, out_specs=out_specs, check_vma=False
    )
```

```python
import functools

import jax
import jax.numpy as jnp
from jax import lax
from jax.experimental import pallas as pl
from jax.experimental.pallas import tpu as pltpu
from jax.sharding import PartitionSpec as P

LEFT_CHUNK = 16
RIGHT_CHUNK = 32
VMEM_LIMIT = 48 * 1024 * 1024


def _left_kernel(dep_ref, sector_ref, count_ref, m_ref, x_ref, o_ref):
    base = pl.program_id(0) * LEFT_CHUNK
    n_term, _, rows, _ = o_ref.shape
    for k in range(LEFT_CHUNK):
        slot = dep_ref[base + k]
        prod = jnp.dot(
            m_ref[sector_ref[slot]], x_ref[slot], preferred_element_type=jnp.float32
        )
        prod = jnp.where(slot < count_ref[0], prod, 0.0).astype(o_ref.dtype)
        for p in range(n_term):
            o_ref[p, k] = prod[p * rows:(p + 1) * rows]


def apply_left(blocks, tiles, dep, left_sector, tile_count, n_term):
    n, w, _ = tiles.shape
    rows = w // n_term
    spec = pltpu.PrefetchScalarGridSpec(
        num_scalar_prefetch=3,
        grid=(n // LEFT_CHUNK,),
        in_specs=[
            pl.BlockSpec(blocks.shape, lambda c, *_: (0, 0, 0)),
            pl.BlockSpec(tiles.shape, lambda c, *_: (0, 0, 0)),
        ],
        out_specs=pl.BlockSpec((n_term, LEFT_CHUNK, rows, w), lambda c, *_: (0, c, 0, 0)),
    )
    return pl.pallas_call(
        _left_kernel,
        grid_spec=spec,
        out_shape=jax.ShapeDtypeStruct((n_term, n, rows, w), jnp.bfloat16),
        compiler_params=pltpu.CompilerParams(vmem_limit_bytes=VMEM_LIMIT),
        cost_estimate=pl.CostEstimate(
            flops=2 * n * w * w * w,
            bytes_accessed=2 * (2 * n * w * w + blocks.size),
            transcendentals=0,
        ),
    )(dep, left_sector, tile_count, blocks, tiles)


def _right_kernel(n_term, n_sector, arr_ref, rsel_ref, me_ref, a_ref, rt_ref, o_ref):
    base = pl.program_id(0) * RIGHT_CHUNK
    rows = o_ref.shape[1]
    per_term = a_ref.shape[0] // n_term
    accs = [None] * n_sector
    for k in range(n_term):
        origin = lax.rem(me_ref[0] + (n_term - k), n_term) * per_term
        lhs = jnp.concatenate(
            [a_ref[origin + arr_ref[base + q]] for q in range(RIGHT_CHUNK)], axis=0
        )
        for sector in range(n_sector):
            part = jnp.dot(
                lhs, rt_ref[k * n_sector + sector], preferred_element_type=jnp.float32
            )
            accs[sector] = part if accs[sector] is None else accs[sector] + part
    for q in range(RIGHT_CHUNK):
        chosen = rsel_ref[base + q]
        out = accs[n_sector - 1][q * rows:(q + 1) * rows]
        for sector in range(n_sector - 1):
            out = jnp.where(chosen == sector, accs[sector][q * rows:(q + 1) * rows], out)
        o_ref[q] = out.astype(o_ref.dtype)


def apply_right(incoming, right_t, arr, rsel, me, n_term, n_sector):
    total, rows, w = incoming.shape
    n = arr.shape[0]
    spec = pltpu.PrefetchScalarGridSpec(
        num_scalar_prefetch=3,
        grid=(n // RIGHT_CHUNK,),
        in_specs=[
            pl.BlockSpec(incoming.shape, lambda c, *_: (0, 0, 0)),
            pl.BlockSpec(right_t.shape, lambda c, *_: (0, 0, 0)),
        ],
        out_specs=pl.BlockSpec((RIGHT_CHUNK, rows, w), lambda c, *_: (c, 0, 0)),
    )
    return pl.pallas_call(
        functools.partial(_right_kernel, n_term, n_sector),
        grid_spec=spec,
        out_shape=jax.ShapeDtypeStruct((n, rows, w), jnp.bfloat16),
        compiler_params=pltpu.CompilerParams(vmem_limit_bytes=VMEM_LIMIT),
        cost_estimate=pl.CostEstimate(
            flops=2 * n_sector * total * rows * w * w,
            bytes_accessed=2 * (total * rows * w + right_t.size + n * rows * w),
            transcendentals=0,
        ),
    )(arr, rsel, me, incoming, right_t)


def on_device(
    vectors, left_env, right_env, left_sector, right_sector, tile_count, departure, arrival
):
    n_term = lax.axis_size("term")
    me = lax.axis_index("term")
    n_vecs, tiles_dev, width, _ = vectors.shape
    n_sector = left_env.shape[1]
    rows = width // n_term

    own_right_t = jnp.swapaxes(right_env[0], 1, 2)
    right_parts = [own_right_t]
    for k in range(1, n_term):
        perm = [(i, (i + k) % n_term) for i in range(n_term)]
        right_parts.append(lax.ppermute(own_right_t, "term", perm))
    right_t = jnp.stack(right_parts).reshape(n_term * n_sector, width, width)
    me_arr = jnp.reshape(me, (1,)).astype(jnp.int32)

    outs = []
    for v in range(n_vecs):
        outgoing = apply_left(
            left_env[0], vectors[v], departure[0], left_sector[0], tile_count, n_term
        )
        incoming = lax.all_to_all(
            outgoing.reshape(n_term * tiles_dev, rows, width),
            ("term", "sec"), split_axis=0, concat_axis=0, tiled=True,
        )
        outs.append(
            apply_right(incoming, right_t, arrival[0], right_sector[0], me_arr, n_term, n_sector)
        )
    return jnp.stack(outs)


def solution(mesh):
    in_specs = (
        P(None, "sec", None, None),
        P("term", "sec", None, None),
        P("term", "sec", None, None),
        P("sec", None),
        P("sec", None),
        P("sec"),
        P("sec", None),
        P("sec", None),
    )
    out_specs = P(None, "sec", "term", None)
    return jax.shard_map(
        on_device, mesh=mesh, in_specs=in_specs, out_specs=out_specs, check_vma=False
    )
```

```python
import functools

import jax
import jax.numpy as jnp
from jax import lax
from jax.experimental import pallas as pl
from jax.experimental.pallas import tpu as pltpu
from jax.sharding import PartitionSpec as P

LEFT_CHUNK = 16
RIGHT_CHUNK = 16
VMEM_LIMIT = 48 * 1024 * 1024


def _left_kernel(dep_ref, sector_ref, count_ref, m_ref, x_ref, o_ref):
    base = pl.program_id(0) * LEFT_CHUNK
    n_term, _, rows, _ = o_ref.shape
    for k in range(LEFT_CHUNK):
        slot = dep_ref[base + k]
        prod = jnp.dot(
            m_ref[sector_ref[slot]], x_ref[slot], preferred_element_type=jnp.float32
        )
        prod = jnp.where(slot < count_ref[0], prod, 0.0).astype(o_ref.dtype)
        for p in range(n_term):
            o_ref[p, k] = prod[p * rows:(p + 1) * rows]


def apply_left(blocks, tiles, dep, left_sector, tile_count, n_term):
    n, w, _ = tiles.shape
    rows = w // n_term
    spec = pltpu.PrefetchScalarGridSpec(
        num_scalar_prefetch=3,
        grid=(n // LEFT_CHUNK,),
        in_specs=[
            pl.BlockSpec(blocks.shape, lambda c, *_: (0, 0, 0)),
            pl.BlockSpec(tiles.shape, lambda c, *_: (0, 0, 0)),
        ],
        out_specs=pl.BlockSpec((n_term, LEFT_CHUNK, rows, w), lambda c, *_: (0, c, 0, 0)),
    )
    return pl.pallas_call(
        _left_kernel,
        grid_spec=spec,
        out_shape=jax.ShapeDtypeStruct((n_term, n, rows, w), jnp.bfloat16),
        compiler_params=pltpu.CompilerParams(vmem_limit_bytes=VMEM_LIMIT),
        cost_estimate=pl.CostEstimate(
            flops=2 * n * w * w * w,
            bytes_accessed=2 * (2 * n * w * w + blocks.size),
            transcendentals=0,
        ),
    )(dep, left_sector, tile_count, blocks, tiles)


def _right_kernel(n_term, n_sector, order_ref, ssec_ref, sarr_ref, me_ref, a_ref, rt_ref,
                  o_hbm, obuf, sem):
    c = pl.program_id(0)
    steps = pl.num_programs(0)
    base = c * RIGHT_CHUNK
    rows = obuf.shape[2]
    per_term = a_ref.shape[0] // n_term
    slot = lax.rem(c, 2)

    def writes(step, buf):
        return [
            pltpu.make_async_copy(
                obuf.at[buf, q], o_hbm.at[order_ref[step * RIGHT_CHUNK + q]], sem.at[buf, q]
            )
            for q in range(RIGHT_CHUNK)
        ]

    @pl.when(c >= 2)
    def _():
        for cp in writes(c - 2, slot):
            cp.wait()

    lhs = []
    for k in range(n_term):
        origin = lax.rem(me_ref[0] + (n_term - k), n_term) * per_term
        lhs.append(jnp.concatenate(
            [a_ref[origin + sarr_ref[base + q]] for q in range(RIGHT_CHUNK)], axis=0
        ))
    first = ssec_ref[base]
    mixed = first != ssec_ref[base + RIGHT_CHUNK - 1]

    @pl.when(jnp.logical_not(mixed))
    def _():
        acc = None
        for k in range(n_term):
            part = jnp.dot(
                lhs[k], rt_ref[k * n_sector + first], preferred_element_type=jnp.float32
            )
            acc = part if acc is None else acc + part
        for q in range(RIGHT_CHUNK):
            obuf[slot, q] = acc[q * rows:(q + 1) * rows].astype(obuf.dtype)

    @pl.when(mixed)
    def _():
        accs = [None] * n_sector
        for k in range(n_term):
            for sector in range(n_sector):
                part = jnp.dot(
                    lhs[k], rt_ref[k * n_sector + sector], preferred_element_type=jnp.float32
                )
                accs[sector] = part if accs[sector] is None else accs[sector] + part
        for q in range(RIGHT_CHUNK):
            chosen = ssec_ref[base + q]
            out = accs[n_sector - 1][q * rows:(q + 1) * rows]
            for sector in range(n_sector - 1):
                out = jnp.where(chosen == sector, accs[sector][q * rows:(q + 1) * rows], out)
            obuf[slot, q] = out.astype(obuf.dtype)

    for cp in writes(c, slot):
        cp.start()

    @pl.when(c == steps - 1)
    def _():
        @pl.when(c >= 1)
        def _():
            for cp in writes(c - 1, 1 - slot):
                cp.wait()
        for cp in writes(c, slot):
            cp.wait()


def apply_right(incoming, right_t, arr, rsel, me, n_term, n_sector):
    total, rows, w = incoming.shape
    n = arr.shape[0]
    idx = jnp.arange(n, dtype=jnp.int32)
    before = (rsel[None, :] < rsel[:, None]) | (
        (rsel[None, :] == rsel[:, None]) & (idx[None, :] < idx[:, None])
    )
    position = jnp.sum(before.astype(jnp.int32), axis=1)
    order = jnp.sum(jnp.where(position[None, :] == idx[:, None], idx[None, :], 0), axis=1)
    ssec = jnp.take(rsel, order)
    sarr = jnp.take(arr, order)
    spec = pltpu.PrefetchScalarGridSpec(
        num_scalar_prefetch=4,
        grid=(n // RIGHT_CHUNK,),
        in_specs=[
            pl.BlockSpec(incoming.shape, lambda c, *_: (0, 0, 0)),
            pl.BlockSpec(right_t.shape, lambda c, *_: (0, 0, 0)),
        ],
        out_specs=pl.BlockSpec(memory_space=pl.ANY),
        scratch_shapes=[
            pltpu.VMEM((2, RIGHT_CHUNK, rows, w), jnp.bfloat16),
            pltpu.SemaphoreType.DMA((2, RIGHT_CHUNK)),
        ],
    )
    return pl.pallas_call(
        functools.partial(_right_kernel, n_term, n_sector),
        grid_spec=spec,
        out_shape=jax.ShapeDtypeStruct((n, rows, w), jnp.bfloat16),
        compiler_params=pltpu.CompilerParams(
            vmem_limit_bytes=VMEM_LIMIT, dimension_semantics=("arbitrary",)
        ),
        cost_estimate=pl.CostEstimate(
            flops=2 * total * rows * w * w,
            bytes_accessed=2 * (total * rows * w + right_t.size + n * rows * w),
            transcendentals=0,
        ),
    )(order, ssec, sarr, me, incoming, right_t)


def on_device(
    vectors, left_env, right_env, left_sector, right_sector, tile_count, departure, arrival
):
    n_term = lax.axis_size("term")
    me = lax.axis_index("term")
    n_vecs, tiles_dev, width, _ = vectors.shape
    n_sector = left_env.shape[1]
    rows = width // n_term

    own_right_t = jnp.swapaxes(right_env[0], 1, 2)
    right_parts = [own_right_t]
    for k in range(1, n_term):
        perm = [(i, (i + k) % n_term) for i in range(n_term)]
        right_parts.append(lax.ppermute(own_right_t, "term", perm))
    right_t = jnp.stack(right_parts).reshape(n_term * n_sector, width, width)
    me_arr = jnp.reshape(me, (1,)).astype(jnp.int32)

    outs = []
    for v in range(n_vecs):
        outgoing = apply_left(
            left_env[0], vectors[v], departure[0], left_sector[0], tile_count, n_term
        )
        incoming = lax.all_to_all(
            outgoing.reshape(n_term * tiles_dev, rows, width),
            ("term", "sec"), split_axis=0, concat_axis=0, tiled=True,
        )
        outs.append(
            apply_right(incoming, right_t, arrival[0], right_sector[0], me_arr, n_term, n_sector)
        )
    return jnp.stack(outs)


def solution(mesh):
    in_specs = (
        P(None, "sec", None, None),
        P("term", "sec", None, None),
        P("term", "sec", None, None),
        P("sec", None),
        P("sec", None),
        P("sec"),
        P("sec", None),
        P("sec", None),
    )
    out_specs = P(None, "sec", "term", None)
    return jax.shard_map(
        on_device, mesh=mesh, in_specs=in_specs, out_specs=out_specs, check_vma=False
    )
```

```python
import functools

import jax
import jax.numpy as jnp
from jax import lax
from jax.experimental import pallas as pl
from jax.experimental.pallas import tpu as pltpu
from jax.sharding import PartitionSpec as P

LEFT_CHUNK = 16
RIGHT_CHUNK = 16
VMEM_LIMIT = 48 * 1024 * 1024


def _left_kernel(n_tiles, meta_ref, m_ref, x_ref, o_hbm, obuf, sem):
    c = pl.program_id(0)
    steps = pl.num_programs(0)
    base = c * LEFT_CHUNK
    n_term, _, rows, _ = obuf.shape[1:]
    slot = lax.rem(c, 2)

    def writes(step, buf):
        return [
            pltpu.make_async_copy(
                obuf.at[buf, :, q], o_hbm.at[:, meta_ref[step * LEFT_CHUNK + q]], sem.at[buf, q]
            )
            for q in range(LEFT_CHUNK)
        ]

    @pl.when(c >= 2)
    def _():
        for cp in writes(c - 2, slot):
            cp.wait()

    for q in range(LEFT_CHUNK):
        tile = base + q
        prod = jnp.dot(
            m_ref[meta_ref[n_tiles + tile]], x_ref[q], preferred_element_type=jnp.float32
        )
        prod = jnp.where(tile < meta_ref[2 * n_tiles], prod, 0.0).astype(obuf.dtype)
        for p in range(n_term):
            obuf[slot, p, q] = prod[p * rows:(p + 1) * rows]

    for cp in writes(c, slot):
        cp.start()

    @pl.when(c == steps - 1)
    def _():
        @pl.when(c >= 1)
        def _():
            for cp in writes(c - 1, 1 - slot):
                cp.wait()
        for cp in writes(c, slot):
            cp.wait()


def apply_left(blocks, tiles, dep, left_sector, tile_count, n_term):
    n, w, _ = tiles.shape
    rows = w // n_term
    idx = jnp.arange(n, dtype=jnp.int32)
    position = jnp.sum(jnp.where(dep[None, :] == idx[:, None], idx[None, :], 0), axis=1)
    meta = jnp.concatenate([position, left_sector, tile_count])
    spec = pltpu.PrefetchScalarGridSpec(
        num_scalar_prefetch=1,
        grid=(n // LEFT_CHUNK,),
        in_specs=[
            pl.BlockSpec(blocks.shape, lambda c, *_: (0, 0, 0)),
            pl.BlockSpec((LEFT_CHUNK, w, w), lambda c, *_: (c, 0, 0)),
        ],
        out_specs=pl.BlockSpec(memory_space=pl.ANY),
        scratch_shapes=[
            pltpu.VMEM((2, n_term, LEFT_CHUNK, rows, w), jnp.bfloat16),
            pltpu.SemaphoreType.DMA((2, LEFT_CHUNK)),
        ],
    )
    return pl.pallas_call(
        functools.partial(_left_kernel, n),
        grid_spec=spec,
        out_shape=jax.ShapeDtypeStruct((n_term, n, rows, w), jnp.bfloat16),
        compiler_params=pltpu.CompilerParams(
            vmem_limit_bytes=VMEM_LIMIT, dimension_semantics=("arbitrary",)
        ),
        cost_estimate=pl.CostEstimate(
            flops=2 * n * w * w * w,
            bytes_accessed=2 * (2 * n * w * w + blocks.size),
            transcendentals=0,
        ),
    )(meta, blocks, tiles)


def _right_kernel(n_term, n_sector, order_ref, ssec_ref, sarr_ref, me_ref, a_ref, rt_ref,
                  o_hbm, obuf, sem):
    c = pl.program_id(0)
    steps = pl.num_programs(0)
    base = c * RIGHT_CHUNK
    rows = obuf.shape[2]
    per_term = a_ref.shape[0] // n_term
    slot = lax.rem(c, 2)

    def writes(step, buf):
        return [
            pltpu.make_async_copy(
                obuf.at[buf, q], o_hbm.at[order_ref[step * RIGHT_CHUNK + q]], sem.at[buf, q]
            )
            for q in range(RIGHT_CHUNK)
        ]

    @pl.when(c >= 2)
    def _():
        for cp in writes(c - 2, slot):
            cp.wait()

    lhs = []
    for k in range(n_term):
        origin = lax.rem(me_ref[0] + (n_term - k), n_term) * per_term
        lhs.append(jnp.concatenate(
            [a_ref[origin + sarr_ref[base + q]] for q in range(RIGHT_CHUNK)], axis=0
        ))
    first = ssec_ref[base]
    mixed = first != ssec_ref[base + RIGHT_CHUNK - 1]

    @pl.when(jnp.logical_not(mixed))
    def _():
        acc = None
        for k in range(n_term):
            part = jnp.dot(
                lhs[k], rt_ref[k * n_sector + first], preferred_element_type=jnp.float32
            )
            acc = part if acc is None else acc + part
        for q in range(RIGHT_CHUNK):
            obuf[slot, q] = acc[q * rows:(q + 1) * rows].astype(obuf.dtype)

    @pl.when(mixed)
    def _():
        accs = [None] * n_sector
        for k in range(n_term):
            for sector in range(n_sector):
                part = jnp.dot(
                    lhs[k], rt_ref[k * n_sector + sector], preferred_element_type=jnp.float32
                )
                accs[sector] = part if accs[sector] is None else accs[sector] + part
        for q in range(RIGHT_CHUNK):
            chosen = ssec_ref[base + q]
            out = accs[n_sector - 1][q * rows:(q + 1) * rows]
            for sector in range(n_sector - 1):
                out = jnp.where(chosen == sector, accs[sector][q * rows:(q + 1) * rows], out)
            obuf[slot, q] = out.astype(obuf.dtype)

    for cp in writes(c, slot):
        cp.start()

    @pl.when(c == steps - 1)
    def _():
        @pl.when(c >= 1)
        def _():
            for cp in writes(c - 1, 1 - slot):
                cp.wait()
        for cp in writes(c, slot):
            cp.wait()


def apply_right(incoming, right_t, arr, rsel, me, n_term, n_sector):
    total, rows, w = incoming.shape
    n = arr.shape[0]
    idx = jnp.arange(n, dtype=jnp.int32)
    before = (rsel[None, :] < rsel[:, None]) | (
        (rsel[None, :] == rsel[:, None]) & (idx[None, :] < idx[:, None])
    )
    position = jnp.sum(before.astype(jnp.int32), axis=1)
    order = jnp.sum(jnp.where(position[None, :] == idx[:, None], idx[None, :], 0), axis=1)
    ssec = jnp.take(rsel, order)
    sarr = jnp.take(arr, order)
    spec = pltpu.PrefetchScalarGridSpec(
        num_scalar_prefetch=4,
        grid=(n // RIGHT_CHUNK,),
        in_specs=[
            pl.BlockSpec(incoming.shape, lambda c, *_: (0, 0, 0)),
            pl.BlockSpec(right_t.shape, lambda c, *_: (0, 0, 0)),
        ],
        out_specs=pl.BlockSpec(memory_space=pl.ANY),
        scratch_shapes=[
            pltpu.VMEM((2, RIGHT_CHUNK, rows, w), jnp.bfloat16),
            pltpu.SemaphoreType.DMA((2, RIGHT_CHUNK)),
        ],
    )
    return pl.pallas_call(
        functools.partial(_right_kernel, n_term, n_sector),
        grid_spec=spec,
        out_shape=jax.ShapeDtypeStruct((n, rows, w), jnp.bfloat16),
        compiler_params=pltpu.CompilerParams(
            vmem_limit_bytes=VMEM_LIMIT, dimension_semantics=("arbitrary",)
        ),
        cost_estimate=pl.CostEstimate(
            flops=2 * total * rows * w * w,
            bytes_accessed=2 * (total * rows * w + right_t.size + n * rows * w),
            transcendentals=0,
        ),
    )(order, ssec, sarr, me, incoming, right_t)


def on_device(
    vectors, left_env, right_env, left_sector, right_sector, tile_count, departure, arrival
):
    n_term = lax.axis_size("term")
    me = lax.axis_index("term")
    n_vecs, tiles_dev, width, _ = vectors.shape
    n_sector = left_env.shape[1]
    rows = width // n_term

    own_right_t = jnp.swapaxes(right_env[0], 1, 2)
    right_parts = [own_right_t]
    for k in range(1, n_term):
        perm = [(i, (i + k) % n_term) for i in range(n_term)]
        right_parts.append(lax.ppermute(own_right_t, "term", perm))
    right_t = jnp.stack(right_parts).reshape(n_term * n_sector, width, width)
    me_arr = jnp.reshape(me, (1,)).astype(jnp.int32)

    outs = []
    for v in range(n_vecs):
        outgoing = apply_left(
            left_env[0], vectors[v], departure[0], left_sector[0], tile_count, n_term
        )
        incoming = lax.all_to_all(
            outgoing.reshape(n_term * tiles_dev, rows, width),
            ("term", "sec"), split_axis=0, concat_axis=0, tiled=True,
        )
        outs.append(
            apply_right(incoming, right_t, arrival[0], right_sector[0], me_arr, n_term, n_sector)
        )
    return jnp.stack(outs)


def solution(mesh):
    in_specs = (
        P(None, "sec", None, None),
        P("term", "sec", None, None),
        P("term", "sec", None, None),
        P("sec", None),
        P("sec", None),
        P("sec"),
        P("sec", None),
        P("sec", None),
    )
    out_specs = P(None, "sec", "term", None)
    return jax.shard_map(
        on_device, mesh=mesh, in_specs=in_specs, out_specs=out_specs, check_vma=False
    )
```

```python
import functools

import jax
import jax.numpy as jnp
from jax import lax
from jax.experimental import pallas as pl
from jax.experimental.pallas import tpu as pltpu
from jax.sharding import PartitionSpec as P

LEFT_CHUNK = 16
RIGHT_CHUNK = 16
VMEM_LIMIT = 48 * 1024 * 1024


def _left_kernel(dep_ref, sector_ref, count_ref, m_ref, x_ref, o_ref):
    base = pl.program_id(0) * LEFT_CHUNK
    for k in range(LEFT_CHUNK):
        slot = dep_ref[base + k]
        prod = jnp.dot(
            m_ref[sector_ref[slot]], x_ref[slot], preferred_element_type=jnp.float32
        )
        o_ref[k] = jnp.where(slot < count_ref[0], prod, 0.0).astype(o_ref.dtype)


def apply_left(stacked, tiles, dep, left_sector, tile_count):
    n, w, _ = tiles.shape
    height = stacked.shape[1]
    spec = pltpu.PrefetchScalarGridSpec(
        num_scalar_prefetch=3,
        grid=(n // LEFT_CHUNK,),
        in_specs=[
            pl.BlockSpec(stacked.shape, lambda c, *_: (0, 0, 0)),
            pl.BlockSpec(tiles.shape, lambda c, *_: (0, 0, 0)),
        ],
        out_specs=pl.BlockSpec((LEFT_CHUNK, height, w), lambda c, *_: (c, 0, 0)),
    )
    return pl.pallas_call(
        _left_kernel,
        grid_spec=spec,
        out_shape=jax.ShapeDtypeStruct((n, height, w), jnp.bfloat16),
        compiler_params=pltpu.CompilerParams(vmem_limit_bytes=VMEM_LIMIT),
        cost_estimate=pl.CostEstimate(
            flops=2 * n * height * w * w,
            bytes_accessed=2 * (n * w * w + n * height * w + stacked.size),
            transcendentals=0,
        ),
    )(dep, left_sector, tile_count, stacked, tiles)


def _right_kernel(n_term, n_sector, order_ref, ssec_ref, sarr_ref, me_ref, a_ref, rt_ref,
                  o_hbm, obuf, sem):
    c = pl.program_id(0)
    steps = pl.num_programs(0)
    base = c * RIGHT_CHUNK
    rows = obuf.shape[2]
    slot = lax.rem(c, 2)

    def writes(step, buf):
        return [
            pltpu.make_async_copy(
                obuf.at[buf, q], o_hbm.at[order_ref[step * RIGHT_CHUNK + q]], sem.at[buf, q]
            )
            for q in range(RIGHT_CHUNK)
        ]

    @pl.when(c >= 2)
    def _():
        for cp in writes(c - 2, slot):
            cp.wait()

    n_peer = a_ref.shape[0]
    shifts = [lax.rem(me_ref[0] + n_peer - sarr_ref[base + q], n_peer) for q in range(RIGHT_CHUNK)]
    lhs = []
    for k in range(n_term):
        lhs.append(jnp.concatenate(
            [a_ref[shifts[q], pl.ds(k * rows, rows), :] for q in range(RIGHT_CHUNK)], axis=0
        ))
    first = ssec_ref[base]
    mixed = first != ssec_ref[base + RIGHT_CHUNK - 1]

    @pl.when(jnp.logical_not(mixed))
    def _():
        acc = None
        for k in range(n_term):
            part = jnp.dot(
                lhs[k], rt_ref[k * n_sector + first], preferred_element_type=jnp.float32
            )
            acc = part if acc is None else acc + part
        for q in range(RIGHT_CHUNK):
            obuf[slot, q] = acc[q * rows:(q + 1) * rows].astype(obuf.dtype)

    @pl.when(mixed)
    def _():
        accs = [None] * n_sector
        for k in range(n_term):
            for sector in range(n_sector):
                part = jnp.dot(
                    lhs[k], rt_ref[k * n_sector + sector], preferred_element_type=jnp.float32
                )
                accs[sector] = part if accs[sector] is None else accs[sector] + part
        for q in range(RIGHT_CHUNK):
            chosen = ssec_ref[base + q]
            out = accs[n_sector - 1][q * rows:(q + 1) * rows]
            for sector in range(n_sector - 1):
                out = jnp.where(chosen == sector, accs[sector][q * rows:(q + 1) * rows], out)
            obuf[slot, q] = out.astype(obuf.dtype)

    for cp in writes(c, slot):
        cp.start()

    @pl.when(c == steps - 1)
    def _():
        @pl.when(c >= 1)
        def _():
            for cp in writes(c - 1, 1 - slot):
                cp.wait()
        for cp in writes(c, slot):
            cp.wait()


def apply_right(incoming, right_t, arr, rsel, me, n_term, n_sector):
    total, height, w = incoming.shape
    rows = height // n_term
    n = arr.shape[0]
    idx = jnp.arange(n, dtype=jnp.int32)
    before = (rsel[None, :] < rsel[:, None]) | (
        (rsel[None, :] == rsel[:, None]) & (idx[None, :] < idx[:, None])
    )
    position = jnp.sum(before.astype(jnp.int32), axis=1)
    order = jnp.sum(jnp.where(position[None, :] == idx[:, None], idx[None, :], 0), axis=1)
    ssec = jnp.take(rsel, order)
    sarr = jnp.take(arr, order)
    spec = pltpu.PrefetchScalarGridSpec(
        num_scalar_prefetch=4,
        grid=(n // RIGHT_CHUNK,),
        in_specs=[
            pl.BlockSpec(incoming.shape, lambda c, *_: (0, 0, 0)),
            pl.BlockSpec(right_t.shape, lambda c, *_: (0, 0, 0)),
        ],
        out_specs=pl.BlockSpec(memory_space=pl.ANY),
        scratch_shapes=[
            pltpu.VMEM((2, RIGHT_CHUNK, rows, w), jnp.bfloat16),
            pltpu.SemaphoreType.DMA((2, RIGHT_CHUNK)),
        ],
    )
    return pl.pallas_call(
        functools.partial(_right_kernel, n_term, n_sector),
        grid_spec=spec,
        out_shape=jax.ShapeDtypeStruct((n, rows, w), jnp.bfloat16),
        compiler_params=pltpu.CompilerParams(
            vmem_limit_bytes=VMEM_LIMIT, dimension_semantics=("arbitrary",)
        ),
        cost_estimate=pl.CostEstimate(
            flops=2 * total * height * w * w,
            bytes_accessed=2 * (total * height * w + right_t.size + n * rows * w),
            transcendentals=0,
        ),
    )(order, ssec, sarr, me, incoming, right_t)


def on_device(
    vectors, left_env, right_env, left_sector, right_sector, tile_count, departure, arrival
):
    n_term = lax.axis_size("term")
    n_peer = lax.axis_size("sec")
    me = lax.axis_index("term")
    me_sec = lax.axis_index("sec")
    n_vecs, tiles_dev, width, _ = vectors.shape
    n_sector = left_env.shape[1]
    rows = width // n_term

    own_left = left_env[0]
    own_right_t = jnp.swapaxes(right_env[0], 1, 2)
    left_parts = [lax.dynamic_slice_in_dim(own_left, me * rows, rows, axis=1)]
    right_parts = [own_right_t]
    for k in range(1, n_term):
        perm = [(i, (i + k) % n_term) for i in range(n_term)]
        dest = (me + k) % n_term
        send = lax.dynamic_slice_in_dim(own_left, dest * rows, rows, axis=1)
        left_parts.append(lax.ppermute(send, "term", perm))
        right_parts.append(lax.ppermute(own_right_t, "term", perm))
    stacked = jnp.concatenate(left_parts, axis=1)
    right_t = jnp.stack(right_parts).reshape(n_term * n_sector, width, width)
    me_arr = jnp.reshape(me_sec, (1,)).astype(jnp.int32)

    outs = []
    for v in range(n_vecs):
        outgoing = apply_left(stacked, vectors[v], departure[0], left_sector[0], tile_count)
        incoming = lax.dynamic_update_slice_in_dim(
            jnp.zeros_like(outgoing), lax.dynamic_slice_in_dim(outgoing, me_sec, 1), 0, axis=0
        )
        for k in range(1, n_peer):
            perm = [(i, (i + k) % n_peer) for i in range(n_peer)]
            piece = lax.dynamic_slice_in_dim(outgoing, (me_sec + k) % n_peer, 1)
            incoming = lax.dynamic_update_slice_in_dim(
                incoming, lax.ppermute(piece, "sec", perm), k, axis=0
            )
        outs.append(
            apply_right(incoming, right_t, arrival[0], right_sector[0], me_arr, n_term, n_sector)
        )
    return jnp.stack(outs)


def solution(mesh):
    in_specs = (
        P(None, "sec", None, None),
        P("term", "sec", None, None),
        P("term", "sec", None, None),
        P("sec", None),
        P("sec", None),
        P("sec"),
        P("sec", None),
        P("sec", None),
    )
    out_specs = P(None, "sec", "term", None)
    return jax.shard_map(
        on_device, mesh=mesh, in_specs=in_specs, out_specs=out_specs, check_vma=False
    )
```

```python
import functools

import jax
import jax.numpy as jnp
from jax import lax
from jax.experimental import pallas as pl
from jax.experimental.pallas import tpu as pltpu
from jax.sharding import PartitionSpec as P

LEFT_CHUNK = 32
RIGHT_CHUNK = 32
VMEM_LIMIT = 48 * 1024 * 1024


def _left_kernel(dep_ref, sector_ref, count_ref, m_ref, x_ref, o_ref):
    base = pl.program_id(0) * LEFT_CHUNK
    n_term, _, rows, _ = o_ref.shape
    for k in range(LEFT_CHUNK):
        slot = dep_ref[base + k]
        prod = jnp.dot(
            m_ref[sector_ref[slot]], x_ref[slot], preferred_element_type=jnp.float32
        )
        prod = jnp.where(slot < count_ref[0], prod, 0.0).astype(o_ref.dtype)
        for p in range(n_term):
            o_ref[p, k] = prod[p * rows:(p + 1) * rows]


def apply_left(blocks, tiles, dep, left_sector, tile_count, n_term):
    n, w, _ = tiles.shape
    rows = w // n_term
    spec = pltpu.PrefetchScalarGridSpec(
        num_scalar_prefetch=3,
        grid=(n // LEFT_CHUNK,),
        in_specs=[
            pl.BlockSpec(blocks.shape, lambda c, *_: (0, 0, 0)),
            pl.BlockSpec(tiles.shape, lambda c, *_: (0, 0, 0)),
        ],
        out_specs=pl.BlockSpec((n_term, LEFT_CHUNK, rows, w), lambda c, *_: (0, c, 0, 0)),
    )
    return pl.pallas_call(
        _left_kernel,
        grid_spec=spec,
        out_shape=jax.ShapeDtypeStruct((n_term, n, rows, w), jnp.bfloat16),
        compiler_params=pltpu.CompilerParams(vmem_limit_bytes=VMEM_LIMIT),
        cost_estimate=pl.CostEstimate(
            flops=2 * n * w * w * w,
            bytes_accessed=2 * (2 * n * w * w + blocks.size),
            transcendentals=0,
        ),
    )(dep, left_sector, tile_count, blocks, tiles)


def _right_kernel(n_term, n_sector, order_ref, ssec_ref, sarr_ref, me_ref, a_ref, rt_ref,
                  o_hbm, obuf, sem):
    c = pl.program_id(0)
    steps = pl.num_programs(0)
    base = c * RIGHT_CHUNK
    rows = obuf.shape[2]
    per_term = a_ref.shape[0] // n_term
    slot = lax.rem(c, 2)

    def writes(step, buf):
        return [
            pltpu.make_async_copy(
                obuf.at[buf, q], o_hbm.at[order_ref[step * RIGHT_CHUNK + q]], sem.at[buf, q]
            )
            for q in range(RIGHT_CHUNK)
        ]

    @pl.when(c >= 2)
    def _():
        for cp in writes(c - 2, slot):
            cp.wait()

    lhs = []
    for k in range(n_term):
        origin = lax.rem(me_ref[0] + (n_term - k), n_term) * per_term
        lhs.append(jnp.concatenate(
            [a_ref[origin + sarr_ref[base + q]] for q in range(RIGHT_CHUNK)], axis=0
        ))
    first = ssec_ref[base]
    mixed = first != ssec_ref[base + RIGHT_CHUNK - 1]

    @pl.when(jnp.logical_not(mixed))
    def _():
        acc = None
        for k in range(n_term):
            part = jnp.dot(
                lhs[k], rt_ref[k * n_sector + first], preferred_element_type=jnp.float32
            )
            acc = part if acc is None else acc + part
        for q in range(RIGHT_CHUNK):
            obuf[slot, q] = acc[q * rows:(q + 1) * rows].astype(obuf.dtype)

    @pl.when(mixed)
    def _():
        accs = [None] * n_sector
        for k in range(n_term):
            for sector in range(n_sector):
                part = jnp.dot(
                    lhs[k], rt_ref[k * n_sector + sector], preferred_element_type=jnp.float32
                )
                accs[sector] = part if accs[sector] is None else accs[sector] + part
        for q in range(RIGHT_CHUNK):
            chosen = ssec_ref[base + q]
            out = accs[n_sector - 1][q * rows:(q + 1) * rows]
            for sector in range(n_sector - 1):
                out = jnp.where(chosen == sector, accs[sector][q * rows:(q + 1) * rows], out)
            obuf[slot, q] = out.astype(obuf.dtype)

    for cp in writes(c, slot):
        cp.start()

    @pl.when(c == steps - 1)
    def _():
        @pl.when(c >= 1)
        def _():
            for cp in writes(c - 1, 1 - slot):
                cp.wait()
        for cp in writes(c, slot):
            cp.wait()


def apply_right(incoming, right_t, arr, rsel, me, n_term, n_sector):
    total, rows, w = incoming.shape
    n = arr.shape[0]
    idx = jnp.arange(n, dtype=jnp.int32)
    before = (rsel[None, :] < rsel[:, None]) | (
        (rsel[None, :] == rsel[:, None]) & (idx[None, :] < idx[:, None])
    )
    position = jnp.sum(before.astype(jnp.int32), axis=1)
    order = jnp.sum(jnp.where(position[None, :] == idx[:, None], idx[None, :], 0), axis=1)
    ssec = jnp.take(rsel, order)
    sarr = jnp.take(arr, order)
    spec = pltpu.PrefetchScalarGridSpec(
        num_scalar_prefetch=4,
        grid=(n // RIGHT_CHUNK,),
        in_specs=[
            pl.BlockSpec(incoming.shape, lambda c, *_: (0, 0, 0)),
            pl.BlockSpec(right_t.shape, lambda c, *_: (0, 0, 0)),
        ],
        out_specs=pl.BlockSpec(memory_space=pl.ANY),
        scratch_shapes=[
            pltpu.VMEM((2, RIGHT_CHUNK, rows, w), jnp.bfloat16),
            pltpu.SemaphoreType.DMA((2, RIGHT_CHUNK)),
        ],
    )
    return pl.pallas_call(
        functools.partial(_right_kernel, n_term, n_sector),
        grid_spec=spec,
        out_shape=jax.ShapeDtypeStruct((n, rows, w), jnp.bfloat16),
        compiler_params=pltpu.CompilerParams(
            vmem_limit_bytes=VMEM_LIMIT, dimension_semantics=("arbitrary",)
        ),
        cost_estimate=pl.CostEstimate(
            flops=2 * total * rows * w * w,
            bytes_accessed=2 * (total * rows * w + right_t.size + n * rows * w),
            transcendentals=0,
        ),
    )(order, ssec, sarr, me, incoming, right_t)


def on_device(
    vectors, left_env, right_env, left_sector, right_sector, tile_count, departure, arrival
):
    n_term = lax.axis_size("term")
    me = lax.axis_index("term")
    n_vecs, tiles_dev, width, _ = vectors.shape
    n_sector = left_env.shape[1]
    rows = width // n_term

    own_right_t = jnp.swapaxes(right_env[0], 1, 2)
    right_parts = [own_right_t]
    for k in range(1, n_term):
        perm = [(i, (i + k) % n_term) for i in range(n_term)]
        right_parts.append(lax.ppermute(own_right_t, "term", perm))
    right_t = jnp.stack(right_parts).reshape(n_term * n_sector, width, width)
    me_arr = jnp.reshape(me, (1,)).astype(jnp.int32)

    outs = []
    for v in range(n_vecs):
        outgoing = apply_left(
            left_env[0], vectors[v], departure[0], left_sector[0], tile_count, n_term
        )
        incoming = lax.all_to_all(
            outgoing.reshape(n_term * tiles_dev, rows, width),
            ("term", "sec"), split_axis=0, concat_axis=0, tiled=True,
        )
        outs.append(
            apply_right(incoming, right_t, arrival[0], right_sector[0], me_arr, n_term, n_sector)
        )
    return jnp.stack(outs)


def solution(mesh):
    in_specs = (
        P(None, "sec", None, None),
        P("term", "sec", None, None),
        P("term", "sec", None, None),
        P("sec", None),
        P("sec", None),
        P("sec"),
        P("sec", None),
        P("sec", None),
    )
    out_specs = P(None, "sec", "term", None)
    return jax.shard_map(
        on_device, mesh=mesh, in_specs=in_specs, out_specs=out_specs, check_vma=False
    )
```

```python
import functools

import jax
import jax.numpy as jnp
from jax import lax
from jax.experimental import pallas as pl
from jax.experimental.pallas import tpu as pltpu
from jax.sharding import PartitionSpec as P

LEFT_CHUNK = 16
RIGHT_CHUNK = 16
VMEM_LIMIT = 48 * 1024 * 1024


def _left_kernel(dep_ref, sector_ref, count_ref, m_ref, x_ref, o_ref):
    base = pl.program_id(0) * LEFT_CHUNK
    _, n_term, rows, _ = o_ref.shape
    for k in range(LEFT_CHUNK):
        slot = dep_ref[base + k]
        prod = jnp.dot(
            m_ref[sector_ref[slot]], x_ref[slot], preferred_element_type=jnp.float32
        )
        prod = jnp.where(slot < count_ref[0], prod, 0.0).astype(o_ref.dtype)
        for p in range(n_term):
            o_ref[k, p] = prod[p * rows:(p + 1) * rows]


def apply_left(blocks, tiles, dep, left_sector, tile_count, n_term):
    n, w, _ = tiles.shape
    rows = w // n_term
    spec = pltpu.PrefetchScalarGridSpec(
        num_scalar_prefetch=3,
        grid=(n // LEFT_CHUNK,),
        in_specs=[
            pl.BlockSpec(blocks.shape, lambda c, *_: (0, 0, 0)),
            pl.BlockSpec(tiles.shape, lambda c, *_: (0, 0, 0)),
        ],
        out_specs=pl.BlockSpec((LEFT_CHUNK, n_term, rows, w), lambda c, *_: (c, 0, 0, 0)),
    )
    return pl.pallas_call(
        _left_kernel,
        grid_spec=spec,
        out_shape=jax.ShapeDtypeStruct((n, n_term, rows, w), jnp.bfloat16),
        compiler_params=pltpu.CompilerParams(vmem_limit_bytes=VMEM_LIMIT),
        cost_estimate=pl.CostEstimate(
            flops=2 * n * w * w * w,
            bytes_accessed=2 * (2 * n * w * w + blocks.size),
            transcendentals=0,
        ),
    )(dep, left_sector, tile_count, blocks, tiles)


def _right_kernel(n_term, n_sector, order_ref, ssec_ref, sarr_ref, me_ref, a_ref, rt_ref,
                  o_hbm, obuf, sem):
    c = pl.program_id(0)
    steps = pl.num_programs(0)
    base = c * RIGHT_CHUNK
    rows = obuf.shape[2]
    slot = lax.rem(c, 2)

    def writes(step, buf):
        return [
            pltpu.make_async_copy(
                obuf.at[buf, q], o_hbm.at[order_ref[step * RIGHT_CHUNK + q]], sem.at[buf, q]
            )
            for q in range(RIGHT_CHUNK)
        ]

    @pl.when(c >= 2)
    def _():
        for cp in writes(c - 2, slot):
            cp.wait()

    lhs = []
    for k in range(n_term):
        origin = lax.rem(me_ref[0] + (n_term - k), n_term)
        lhs.append(jnp.concatenate(
            [a_ref[sarr_ref[base + q] * n_term + origin] for q in range(RIGHT_CHUNK)], axis=0
        ))
    first = ssec_ref[base]
    mixed = first != ssec_ref[base + RIGHT_CHUNK - 1]

    @pl.when(jnp.logical_not(mixed))
    def _():
        acc = None
        for k in range(n_term):
            part = jnp.dot(
                lhs[k], rt_ref[k * n_sector + first], preferred_element_type=jnp.float32
            )
            acc = part if acc is None else acc + part
        for q in range(RIGHT_CHUNK):
            obuf[slot, q] = acc[q * rows:(q + 1) * rows].astype(obuf.dtype)

    @pl.when(mixed)
    def _():
        accs = [None] * n_sector
        for k in range(n_term):
            for sector in range(n_sector):
                part = jnp.dot(
                    lhs[k], rt_ref[k * n_sector + sector], preferred_element_type=jnp.float32
                )
                accs[sector] = part if accs[sector] is None else accs[sector] + part
        for q in range(RIGHT_CHUNK):
            chosen = ssec_ref[base + q]
            out = accs[n_sector - 1][q * rows:(q + 1) * rows]
            for sector in range(n_sector - 1):
                out = jnp.where(chosen == sector, accs[sector][q * rows:(q + 1) * rows], out)
            obuf[slot, q] = out.astype(obuf.dtype)

    for cp in writes(c, slot):
        cp.start()

    @pl.when(c == steps - 1)
    def _():
        @pl.when(c >= 1)
        def _():
            for cp in writes(c - 1, 1 - slot):
                cp.wait()
        for cp in writes(c, slot):
            cp.wait()


def apply_right(incoming, right_t, arr, rsel, me, n_term, n_sector):
    total, rows, w = incoming.shape
    n = arr.shape[0]
    idx = jnp.arange(n, dtype=jnp.int32)
    before = (rsel[None, :] < rsel[:, None]) | (
        (rsel[None, :] == rsel[:, None]) & (idx[None, :] < idx[:, None])
    )
    position = jnp.sum(before.astype(jnp.int32), axis=1)
    order = jnp.sum(jnp.where(position[None, :] == idx[:, None], idx[None, :], 0), axis=1)
    ssec = jnp.take(rsel, order)
    sarr = jnp.take(arr, order)
    spec = pltpu.PrefetchScalarGridSpec(
        num_scalar_prefetch=4,
        grid=(n // RIGHT_CHUNK,),
        in_specs=[
            pl.BlockSpec(incoming.shape, lambda c, *_: (0, 0, 0)),
            pl.BlockSpec(right_t.shape, lambda c, *_: (0, 0, 0)),
        ],
        out_specs=pl.BlockSpec(memory_space=pl.ANY),
        scratch_shapes=[
            pltpu.VMEM((2, RIGHT_CHUNK, rows, w), jnp.bfloat16),
            pltpu.SemaphoreType.DMA((2, RIGHT_CHUNK)),
        ],
    )
    return pl.pallas_call(
        functools.partial(_right_kernel, n_term, n_sector),
        grid_spec=spec,
        out_shape=jax.ShapeDtypeStruct((n, rows, w), jnp.bfloat16),
        compiler_params=pltpu.CompilerParams(
            vmem_limit_bytes=VMEM_LIMIT, dimension_semantics=("arbitrary",)
        ),
        cost_estimate=pl.CostEstimate(
            flops=2 * total * rows * w * w,
            bytes_accessed=2 * (total * rows * w + right_t.size + n * rows * w),
            transcendentals=0,
        ),
    )(order, ssec, sarr, me, incoming, right_t)


def on_device(
    vectors, left_env, right_env, left_sector, right_sector, tile_count, departure, arrival
):
    n_term = lax.axis_size("term")
    me = lax.axis_index("term")
    n_vecs, tiles_dev, width, _ = vectors.shape
    n_sector = left_env.shape[1]
    rows = width // n_term

    own_right_t = jnp.swapaxes(right_env[0], 1, 2)
    right_parts = [own_right_t]
    for k in range(1, n_term):
        perm = [(i, (i + k) % n_term) for i in range(n_term)]
        right_parts.append(lax.ppermute(own_right_t, "term", perm))
    right_t = jnp.stack(right_parts).reshape(n_term * n_sector, width, width)
    me_arr = jnp.reshape(me, (1,)).astype(jnp.int32)

    outs = []
    for v in range(n_vecs):
        outgoing = apply_left(
            left_env[0], vectors[v], departure[0], left_sector[0], tile_count, n_term
        )
        incoming = lax.all_to_all(
            outgoing.reshape(tiles_dev * n_term, rows, width),
            ("sec", "term"), split_axis=0, concat_axis=0, tiled=True,
        )
        outs.append(
            apply_right(incoming, right_t, arrival[0], right_sector[0], me_arr, n_term, n_sector)
        )
    return jnp.stack(outs)


def solution(mesh):
    in_specs = (
        P(None, "sec", None, None),
        P("term", "sec", None, None),
        P("term", "sec", None, None),
        P("sec", None),
        P("sec", None),
        P("sec"),
        P("sec", None),
        P("sec", None),
    )
    out_specs = P(None, "sec", "term", None)
    return jax.shard_map(
        on_device, mesh=mesh, in_specs=in_specs, out_specs=out_specs, check_vma=False
    )
```

```python
import functools

import jax
import jax.numpy as jnp
from jax import lax
from jax.experimental import pallas as pl
from jax.experimental.pallas import tpu as pltpu
from jax.sharding import PartitionSpec as P

LEFT_CHUNK = 16
RIGHT_CHUNK = 16
VMEM_LIMIT = 48 * 1024 * 1024


def _left_kernel(dep_ref, sector_ref, count_ref, m_ref, x_ref, o_ref):
    base = pl.program_id(0) * LEFT_CHUNK
    n_term, _, rows, _ = o_ref.shape
    for k in range(LEFT_CHUNK):
        slot = dep_ref[base + k]
        live = slot < count_ref[0]

        @pl.when(live)
        def _():
            prod = jnp.dot(
                m_ref[sector_ref[slot]], x_ref[slot], preferred_element_type=jnp.float32
            ).astype(o_ref.dtype)
            for p in range(n_term):
                o_ref[p, k] = prod[p * rows:(p + 1) * rows]

        @pl.when(jnp.logical_not(live))
        def _():
            for p in range(n_term):
                o_ref[p, k] = jnp.zeros((rows, o_ref.shape[3]), o_ref.dtype)


def apply_left(blocks, tiles, dep, left_sector, tile_count, n_term):
    n, w, _ = tiles.shape
    rows = w // n_term
    spec = pltpu.PrefetchScalarGridSpec(
        num_scalar_prefetch=3,
        grid=(n // LEFT_CHUNK,),
        in_specs=[
            pl.BlockSpec(blocks.shape, lambda c, *_: (0, 0, 0)),
            pl.BlockSpec(tiles.shape, lambda c, *_: (0, 0, 0)),
        ],
        out_specs=pl.BlockSpec((n_term, LEFT_CHUNK, rows, w), lambda c, *_: (0, c, 0, 0)),
    )
    return pl.pallas_call(
        _left_kernel,
        grid_spec=spec,
        out_shape=jax.ShapeDtypeStruct((n_term, n, rows, w), jnp.bfloat16),
        compiler_params=pltpu.CompilerParams(vmem_limit_bytes=VMEM_LIMIT),
        cost_estimate=pl.CostEstimate(
            flops=2 * n * w * w * w,
            bytes_accessed=2 * (2 * n * w * w + blocks.size),
            transcendentals=0,
        ),
    )(dep, left_sector, tile_count, blocks, tiles)


def _right_kernel(n_term, n_sector, order_ref, ssec_ref, sarr_ref, me_ref, a_ref, rt_ref,
                  o_hbm, obuf, sem):
    c = pl.program_id(0)
    steps = pl.num_programs(0)
    base = c * RIGHT_CHUNK
    rows = obuf.shape[2]
    per_term = a_ref.shape[0] // n_term
    slot = lax.rem(c, 2)

    def writes(step, buf):
        return [
            pltpu.make_async_copy(
                obuf.at[buf, q], o_hbm.at[order_ref[step * RIGHT_CHUNK + q]], sem.at[buf, q]
            )
            for q in range(RIGHT_CHUNK)
        ]

    @pl.when(c >= 2)
    def _():
        for cp in writes(c - 2, slot):
            cp.wait()

    lhs = []
    for k in range(n_term):
        origin = lax.rem(me_ref[0] + (n_term - k), n_term) * per_term
        lhs.append(jnp.concatenate(
            [a_ref[origin + sarr_ref[base + q]] for q in range(RIGHT_CHUNK)], axis=0
        ))
    first = ssec_ref[base]
    mixed = first != ssec_ref[base + RIGHT_CHUNK - 1]

    @pl.when(jnp.logical_not(mixed))
    def _():
        acc = None
        for k in range(n_term):
            part = jnp.dot(
                lhs[k], rt_ref[k * n_sector + first], preferred_element_type=jnp.float32
            )
            acc = part if acc is None else acc + part
        for q in range(RIGHT_CHUNK):
            obuf[slot, q] = acc[q * rows:(q + 1) * rows].astype(obuf.dtype)

    @pl.when(mixed)
    def _():
        accs = [None] * n_sector
        for k in range(n_term):
            for sector in range(n_sector):
                part = jnp.dot(
                    lhs[k], rt_ref[k * n_sector + sector], preferred_element_type=jnp.float32
                )
                accs[sector] = part if accs[sector] is None else accs[sector] + part
        for q in range(RIGHT_CHUNK):
            chosen = ssec_ref[base + q]
            out = accs[n_sector - 1][q * rows:(q + 1) * rows]
            for sector in range(n_sector - 1):
                out = jnp.where(chosen == sector, accs[sector][q * rows:(q + 1) * rows], out)
            obuf[slot, q] = out.astype(obuf.dtype)

    for cp in writes(c, slot):
        cp.start()

    @pl.when(c == steps - 1)
    def _():
        @pl.when(c >= 1)
        def _():
            for cp in writes(c - 1, 1 - slot):
                cp.wait()
        for cp in writes(c, slot):
            cp.wait()


def apply_right(incoming, right_t, arr, rsel, me, n_term, n_sector):
    total, rows, w = incoming.shape
    n = arr.shape[0]
    idx = jnp.arange(n, dtype=jnp.int32)
    before = (rsel[None, :] < rsel[:, None]) | (
        (rsel[None, :] == rsel[:, None]) & (idx[None, :] < idx[:, None])
    )
    position = jnp.sum(before.astype(jnp.int32), axis=1)
    order = jnp.sum(jnp.where(position[None, :] == idx[:, None], idx[None, :], 0), axis=1)
    ssec = jnp.take(rsel, order)
    sarr = jnp.take(arr, order)
    spec = pltpu.PrefetchScalarGridSpec(
        num_scalar_prefetch=4,
        grid=(n // RIGHT_CHUNK,),
        in_specs=[
            pl.BlockSpec(incoming.shape, lambda c, *_: (0, 0, 0)),
            pl.BlockSpec(right_t.shape, lambda c, *_: (0, 0, 0)),
        ],
        out_specs=pl.BlockSpec(memory_space=pl.ANY),
        scratch_shapes=[
            pltpu.VMEM((2, RIGHT_CHUNK, rows, w), jnp.bfloat16),
            pltpu.SemaphoreType.DMA((2, RIGHT_CHUNK)),
        ],
    )
    return pl.pallas_call(
        functools.partial(_right_kernel, n_term, n_sector),
        grid_spec=spec,
        out_shape=jax.ShapeDtypeStruct((n, rows, w), jnp.bfloat16),
        compiler_params=pltpu.CompilerParams(
            vmem_limit_bytes=VMEM_LIMIT, dimension_semantics=("arbitrary",)
        ),
        cost_estimate=pl.CostEstimate(
            flops=2 * total * rows * w * w,
            bytes_accessed=2 * (total * rows * w + right_t.size + n * rows * w),
            transcendentals=0,
        ),
    )(order, ssec, sarr, me, incoming, right_t)


def on_device(
    vectors, left_env, right_env, left_sector, right_sector, tile_count, departure, arrival
):
    n_term = lax.axis_size("term")
    me = lax.axis_index("term")
    n_vecs, tiles_dev, width, _ = vectors.shape
    n_sector = left_env.shape[1]
    rows = width // n_term

    own_right_t = jnp.swapaxes(right_env[0], 1, 2)
    right_parts = [own_right_t]
    for k in range(1, n_term):
        perm = [(i, (i + k) % n_term) for i in range(n_term)]
        right_parts.append(lax.ppermute(own_right_t, "term", perm))
    right_t = jnp.stack(right_parts).reshape(n_term * n_sector, width, width)
    me_arr = jnp.reshape(me, (1,)).astype(jnp.int32)

    outs = []
    for v in range(n_vecs):
        outgoing = apply_left(
            left_env[0], vectors[v], departure[0], left_sector[0], tile_count, n_term
        )
        incoming = lax.all_to_all(
            outgoing.reshape(n_term * tiles_dev, rows, width),
            ("term", "sec"), split_axis=0, concat_axis=0, tiled=True,
        )
        outs.append(
            apply_right(incoming, right_t, arrival[0], right_sector[0], me_arr, n_term, n_sector)
        )
    return jnp.stack(outs)


def solution(mesh):
    in_specs = (
        P(None, "sec", None, None),
        P("term", "sec", None, None),
        P("term", "sec", None, None),
        P("sec", None),
        P("sec", None),
        P("sec"),
        P("sec", None),
        P("sec", None),
    )
    out_specs = P(None, "sec", "term", None)
    return jax.shard_map(
        on_device, mesh=mesh, in_specs=in_specs, out_specs=out_specs, check_vma=False
    )
```

```python
import functools

import jax
import jax.numpy as jnp
from jax import lax
from jax.experimental import pallas as pl
from jax.experimental.pallas import tpu as pltpu
from jax.sharding import PartitionSpec as P

LEFT_CHUNK = 16
RIGHT_CHUNK = 32
VMEM_LIMIT = 48 * 1024 * 1024


def _left_kernel(dep_ref, sector_ref, count_ref, m_ref, x_ref, o_ref):
    base = pl.program_id(0) * LEFT_CHUNK
    n_term, _, rows, _ = o_ref.shape
    for k in range(LEFT_CHUNK):
        slot = dep_ref[base + k]
        prod = jnp.dot(
            m_ref[sector_ref[slot]], x_ref[slot], preferred_element_type=jnp.float32
        )
        prod = jnp.where(slot < count_ref[0], prod, 0.0).astype(o_ref.dtype)
        for p in range(n_term):
            o_ref[p, k] = prod[p * rows:(p + 1) * rows]


def apply_left(blocks, tiles, dep, left_sector, tile_count, n_term):
    n, w, _ = tiles.shape
    rows = w // n_term
    spec = pltpu.PrefetchScalarGridSpec(
        num_scalar_prefetch=3,
        grid=(n // LEFT_CHUNK,),
        in_specs=[
            pl.BlockSpec(blocks.shape, lambda c, *_: (0, 0, 0)),
            pl.BlockSpec(tiles.shape, lambda c, *_: (0, 0, 0)),
        ],
        out_specs=pl.BlockSpec((n_term, LEFT_CHUNK, rows, w), lambda c, *_: (0, c, 0, 0)),
    )
    return pl.pallas_call(
        _left_kernel,
        grid_spec=spec,
        out_shape=jax.ShapeDtypeStruct((n_term, n, rows, w), jnp.bfloat16),
        compiler_params=pltpu.CompilerParams(vmem_limit_bytes=VMEM_LIMIT),
        cost_estimate=pl.CostEstimate(
            flops=2 * n * w * w * w,
            bytes_accessed=2 * (2 * n * w * w + blocks.size),
            transcendentals=0,
        ),
    )(dep, left_sector, tile_count, blocks, tiles)


def _right_kernel(n_term, n_sector, order_ref, ssec_ref, sarr_ref, me_ref, a_ref, rt_ref,
                  o_hbm, obuf, sem):
    c = pl.program_id(0)
    steps = pl.num_programs(0)
    base = c * RIGHT_CHUNK
    rows = obuf.shape[2]
    per_term = a_ref.shape[0] // n_term
    slot = lax.rem(c, 2)

    def writes(step, buf):
        return [
            pltpu.make_async_copy(
                obuf.at[buf, q], o_hbm.at[order_ref[step * RIGHT_CHUNK + q]], sem.at[buf, q]
            )
            for q in range(RIGHT_CHUNK)
        ]

    @pl.when(c >= 2)
    def _():
        for cp in writes(c - 2, slot):
            cp.wait()

    lhs = []
    for k in range(n_term):
        origin = lax.rem(me_ref[0] + (n_term - k), n_term) * per_term
        lhs.append(jnp.concatenate(
            [a_ref[origin + sarr_ref[base + q]] for q in range(RIGHT_CHUNK)], axis=0
        ))
    first = ssec_ref[base]
    mixed = first != ssec_ref[base + RIGHT_CHUNK - 1]

    @pl.when(jnp.logical_not(mixed))
    def _():
        acc = None
        for k in range(n_term):
            part = jnp.dot(
                lhs[k], rt_ref[k * n_sector + first], preferred_element_type=jnp.float32
            )
            acc = part if acc is None else acc + part
        for q in range(RIGHT_CHUNK):
            obuf[slot, q] = acc[q * rows:(q + 1) * rows].astype(obuf.dtype)

    @pl.when(mixed)
    def _():
        accs = [None] * n_sector
        for k in range(n_term):
            for sector in range(n_sector):
                part = jnp.dot(
                    lhs[k], rt_ref[k * n_sector + sector], preferred_element_type=jnp.float32
                )
                accs[sector] = part if accs[sector] is None else accs[sector] + part
        for q in range(RIGHT_CHUNK):
            chosen = ssec_ref[base + q]
            out = accs[n_sector - 1][q * rows:(q + 1) * rows]
            for sector in range(n_sector - 1):
                out = jnp.where(chosen == sector, accs[sector][q * rows:(q + 1) * rows], out)
            obuf[slot, q] = out.astype(obuf.dtype)

    for cp in writes(c, slot):
        cp.start()

    @pl.when(c == steps - 1)
    def _():
        @pl.when(c >= 1)
        def _():
            for cp in writes(c - 1, 1 - slot):
                cp.wait()
        for cp in writes(c, slot):
            cp.wait()


def apply_right(incoming, right_t, arr, rsel, me, n_term, n_sector):
    total, rows, w = incoming.shape
    n = arr.shape[0]
    idx = jnp.arange(n, dtype=jnp.int32)
    before = (rsel[None, :] < rsel[:, None]) | (
        (rsel[None, :] == rsel[:, None]) & (idx[None, :] < idx[:, None])
    )
    position = jnp.sum(before.astype(jnp.int32), axis=1)
    order = jnp.sum(jnp.where(position[None, :] == idx[:, None], idx[None, :], 0), axis=1)
    ssec = jnp.take(rsel, order)
    sarr = jnp.take(arr, order)
    spec = pltpu.PrefetchScalarGridSpec(
        num_scalar_prefetch=4,
        grid=(n // RIGHT_CHUNK,),
        in_specs=[
            pl.BlockSpec(incoming.shape, lambda c, *_: (0, 0, 0)),
            pl.BlockSpec(right_t.shape, lambda c, *_: (0, 0, 0)),
        ],
        out_specs=pl.BlockSpec(memory_space=pl.ANY),
        scratch_shapes=[
            pltpu.VMEM((2, RIGHT_CHUNK, rows, w), jnp.bfloat16),
            pltpu.SemaphoreType.DMA((2, RIGHT_CHUNK)),
        ],
    )
    return pl.pallas_call(
        functools.partial(_right_kernel, n_term, n_sector),
        grid_spec=spec,
        out_shape=jax.ShapeDtypeStruct((n, rows, w), jnp.bfloat16),
        compiler_params=pltpu.CompilerParams(
            vmem_limit_bytes=VMEM_LIMIT, dimension_semantics=("arbitrary",)
        ),
        cost_estimate=pl.CostEstimate(
            flops=2 * total * rows * w * w,
            bytes_accessed=2 * (total * rows * w + right_t.size + n * rows * w),
            transcendentals=0,
        ),
    )(order, ssec, sarr, me, incoming, right_t)


def on_device(
    vectors, left_env, right_env, left_sector, right_sector, tile_count, departure, arrival
):
    n_term = lax.axis_size("term")
    me = lax.axis_index("term")
    n_vecs, tiles_dev, width, _ = vectors.shape
    n_sector = left_env.shape[1]
    rows = width // n_term

    own_right_t = jnp.swapaxes(right_env[0], 1, 2)
    right_parts = [own_right_t]
    for k in range(1, n_term):
        perm = [(i, (i + k) % n_term) for i in range(n_term)]
        right_parts.append(lax.ppermute(own_right_t, "term", perm))
    right_t = jnp.stack(right_parts).reshape(n_term * n_sector, width, width)
    me_arr = jnp.reshape(me, (1,)).astype(jnp.int32)

    outs = []
    for v in range(n_vecs):
        outgoing = apply_left(
            left_env[0], vectors[v], departure[0], left_sector[0], tile_count, n_term
        )
        incoming = lax.all_to_all(
            outgoing.reshape(n_term * tiles_dev, rows, width),
            ("term", "sec"), split_axis=0, concat_axis=0, tiled=True,
        )
        outs.append(
            apply_right(incoming, right_t, arrival[0], right_sector[0], me_arr, n_term, n_sector)
        )
    return jnp.stack(outs)


def solution(mesh):
    in_specs = (
        P(None, "sec", None, None),
        P("term", "sec", None, None),
        P("term", "sec", None, None),
        P("sec", None),
        P("sec", None),
        P("sec"),
        P("sec", None),
        P("sec", None),
    )
    out_specs = P(None, "sec", "term", None)
    return jax.shard_map(
        on_device, mesh=mesh, in_specs=in_specs, out_specs=out_specs, check_vma=False
    )
```
